256 devices in a mesh: dp: 8 (over y, core), expert: 32 (over z, x).
Axes of the slice: x: 4, y: 4, z: 8, core: 2. Of those that a mesh axis runs over, the one named last changes fastest.
Arguments:
- tokens: bfloat16 [4096, 4096], P('expert', 'dp'), may hold values from -6 to 6
- expert_ids: int32 [4096, 8], P('expert'), may hold values from 0 to 63, all different within a row; in each aligned block of 128 rows (0 to 127, 128 to 255, ...) at most 24 rows name the same one
- route_weights: float32 [4096, 8], P('expert'), may hold values from 0.1 to 0.4
- gate_up_weight: bfloat16 [64, 4096, 1536], P('expert', 'dp'), may hold values from -0.09375 to 0.09375
- down_weight: bfloat16 [64, 768, 4096], P('expert', None, 'dp'), may hold values from -0.21875 to 0.21875
- out_grad: bfloat16 [4096, 4096], P('expert', 'dp'), may hold values from -6 to 6
Outputs:
- layer_out: bfloat16 [4096, 4096], P('expert', 'dp')
- token_grad: bfloat16 [4096, 4096], P('expert', 'dp')
- route_grad: float32 [4096, 8], P('expert')
- gate_up_grad: bfloat16 [64, 4096, 1536], P('expert', 'dp')
- down_grad: bfloat16 [64, 768, 4096], P('expert', None, 'dp')
The draws below stay inside these ranges and needn't reach their ends.
Inputs may be any that keep to these rules, and one draw needn't show every extreme that they name: `expert_ids`: each row names 8 different experts. Among the 128 rows of one group no expert is named more than 24 times, and in every draw some group names some expert exactly 24 times.
All inputs are finite; a program needn't handle non-finite values.
Results may differ from the reference program's by a relative error of at most 0.029.
Values may be sent and summed in bfloat16 or wider, within the bound.
No kernel may reach another device: no remote copies, remote signals or barrier semaphores. Data moves between devices by JAX's collectives and lax.ppermute only.
A program may use at most 128 MiB of HBM per device.

```python
import math
import jax
import jax.numpy as jnp
import numpy as np
from jax import lax

D = 4096
FF = 768
TOP = 8
TOK_DEV = 128
EXPERTS = 64
CAP = 24
TOKENS = 4096
N_DP = 8
N_EXPERT = 32


def levels(rng, extent, cuts, least, largest):
    loudness = 1.0
    for position, shards_of in cuts:
        draws = jax.random.uniform(jax.random.fold_in(jax.random.fold_in(rng, 6), position), (shards_of,), jnp.float32, least / len(cuts), largest / len(cuts))
        loudness = loudness * jnp.repeat(jnp.exp(draws), extent[position] // shards_of).reshape((-1,) + (1,) * (len(extent) - 1 - position))
    return loudness


def routed_block(stream_key, own, number, rows, amount, top, limit, lean):
    ranking = jax.random.permutation(stream_key, amount)
    crowded, usual = portions_of(amount, rows * top, limit, lean, True), portions_of(amount, rows * top, limit, lean, False)
    places = jnp.arange(amount)

    def named(tallies, rotation):
        used = int((tallies > 0).sum())
        fixed = max(1, used // 4)
        moved = fixed + (places - fixed + rotation * (used - fixed)) % max(1, amount - fixed)
        return jnp.zeros((amount,), jnp.int32).at[ranking[jnp.where(places < fixed, places, moved)]].set(jnp.asarray(tallies, jnp.int32))

    tallies = jnp.where(number % 4 == 0, named(crowded, number // 4), named(usual, number - number // 4 - 1))
    mixed = jax.random.permutation(jax.random.fold_in(own, 3), amount)
    source_of, receiver = mixed[0:amount // 2 * 2:2], mixed[1:amount // 2 * 2:2]
    margin = jnp.minimum(tallies[source_of] - 1, limit - tallies[receiver]) // 2
    margin = jnp.where((source_of == ranking[0]) | (receiver == ranking[0]) | (tallies[receiver] == 0), 0, jnp.maximum(margin, 0))
    moved = jax.random.randint(jax.random.fold_in(own, 4), (amount // 2,), 0, 1 << 20) % (margin + 1)
    tallies = tallies.at[source_of].add(-moved).at[receiver].add(moved)
    members = jnp.searchsorted(jnp.cumsum(tallies), jnp.arange(rows * top), side="right").astype(jnp.int32)
    grid = members.reshape(top, rows).T
    grid = grid[jax.random.permutation(jax.random.fold_in(own, 1), rows)]
    rotation = jax.random.randint(jax.random.fold_in(own, 2), (rows, 1), 0, top)
    return jnp.take_along_axis(grid, (jnp.arange(top)[None, :] + rotation) % top, axis=1)


def portions_of(amount, total, most, skew, full):
    portions = [(1 << 20) // math.isqrt(standing ** skew) + 1 for standing in range(1, amount + 1)]
    largest = most if full else min(most, max(-(-total // amount), total * portions[0] // sum(portions)))
    least = 1 if total - largest >= amount - 1 else 0
    counts, surplus = [largest] + [least] * (amount - 1), total - largest - least * (amount - 1)
    while surplus > 0:
        movable = [i for i in range(1, amount) if counts[i] < largest] or [i for i in range(1, amount) if counts[i] < most]
        pool, budget = sum([portions[i] for i in movable]), surplus
        for i in movable:
            addition = min(most - counts[i], max(1, budget * portions[i] // pool), surplus)
            counts[i] = counts[i] + addition
            surplus = surplus - addition
    return np.array(counts)


def gaussian(own_key, extent, deviation, reach, cuts=(), held_as=jnp.bfloat16):
    gain = levels(own_key, extent, cuts, -0.22, 0.18) if cuts else 1.0
    array = jax.random.normal(own_key, extent, jnp.float32) * deviation * gain
    return jnp.minimum(jnp.maximum(array, -reach), reach).astype(held_as)


def setup_inputs(seed: int = 0) -> dict:
    key_list = jax.random.split(jax.random.key(seed), 7)
    tokens = gaussian(key_list[0], (TOKENS, D), 1.0, 6.0, ((0, 32), (1, 8)))
    expert_ids_keys = jax.random.split(jax.random.fold_in(key_list[1], 1), TOKENS // TOK_DEV)
    expert_ids_turns = jax.random.permutation(jax.random.fold_in(key_list[1], 3), TOKENS // TOK_DEV)
    expert_ids = jax.vmap(lambda own, number: routed_block(jax.random.fold_in(key_list[1], 2), own, number, TOK_DEV, EXPERTS, TOP, CAP, 2))(expert_ids_keys, expert_ids_turns).reshape((TOKENS, TOP))
    route_weights = jnp.clip(0.1 + 0.3 * jax.random.uniform(key_list[2], (TOKENS, TOP), jnp.float32) ** levels(key_list[2], (TOKENS, TOP), ((0, 32),), -0.2, 0.2), 0.1, 0.4)
    gate_up_weight = gaussian(key_list[3], (EXPERTS, D, 2 * FF), D ** -0.5, 0.09375, ((0, 32), (1, 8)))
    down_weight = gaussian(key_list[4], (EXPERTS, FF, D), FF ** -0.5, 0.21875, ((0, 32), (2, 8)))
    out_grad = gaussian(key_list[5], (TOKENS, D), 1.0, 6.0, ((0, 32), (1, 8)))
    return dict(tokens=tokens, expert_ids=expert_ids, route_weights=route_weights, gate_up_weight=gate_up_weight, down_weight=down_weight, out_grad=out_grad)


def expert_pass(item):
    x_slots, dy_slots, w_gate_up, w_down = item
    row_total = x_slots.shape[0]
    piece_width = D // N_DP
    x_pieces = x_slots.reshape(row_total, N_DP, piece_width).astype(jnp.float32)
    w_pieces = w_gate_up.reshape(N_DP, piece_width, 2 * FF).astype(jnp.float32)
    partials = jnp.einsum('rjk,jkf->jrf', x_pieces, w_pieces)
    preact = jnp.sum(lax.optimization_barrier(partials.astype(jnp.bfloat16)).astype(jnp.float32), axis=0)
    gate_pre = preact[:, :FF]
    up_pre = preact[:, FF:]
    sigmoid_gate = jax.nn.sigmoid(gate_pre)
    activation = gate_pre * sigmoid_gate
    hidden = (activation * up_pre).astype(jnp.bfloat16)
    y_slots = jnp.dot(hidden, w_down, preferred_element_type=jnp.float32).astype(jnp.bfloat16)
    dy_pieces = dy_slots.reshape(row_total, N_DP, piece_width).astype(jnp.float32)
    wd_pieces = w_down.astype(jnp.float32).reshape(FF, N_DP, piece_width)
    grad_parts = jnp.einsum('rjk,fjk->jrf', dy_pieces, wd_pieces)
    hidden_grad = jnp.sum(lax.optimization_barrier(grad_parts.astype(jnp.bfloat16)).astype(jnp.float32), axis=0)
    gate_grad = hidden_grad * up_pre * sigmoid_gate * (1.0 + gate_pre * (1.0 - sigmoid_gate))
    up_grad = hidden_grad * activation
    preact_grad = jnp.concatenate([gate_grad, up_grad], axis=1).astype(jnp.bfloat16)
    x_grad = jnp.dot(preact_grad, w_gate_up.T, preferred_element_type=jnp.float32).astype(jnp.bfloat16)
    gate_up_grad = jnp.dot(x_slots.T, preact_grad, preferred_element_type=jnp.float32).astype(jnp.bfloat16)
    down_grad = jnp.dot(hidden.T, dy_slots, preferred_element_type=jnp.float32).astype(jnp.bfloat16)
    return y_slots, x_grad, gate_up_grad, down_grad


def reference(tokens, expert_ids, route_weights, gate_up_weight, down_weight, out_grad):
    group_total = N_EXPERT
    grouped = expert_ids.reshape(group_total, TOK_DEV * TOP)
    onehot = (grouped[:, :, None] == jnp.arange(EXPERTS, dtype=jnp.int32)[None, None, :]).astype(jnp.int32)
    slot_rank = jnp.sum(onehot * (jnp.cumsum(onehot, axis=1) - 1), axis=2)
    group_ids = jnp.arange(group_total, dtype=jnp.int32)[:, None]
    route_rows = (grouped * (group_total * CAP) + group_ids * CAP + slot_rank).reshape(-1).astype(jnp.int32)
    slot_total = EXPERTS * group_total * CAP
    token_routes = jnp.repeat(tokens, TOP, axis=0)
    x_all = jnp.zeros((slot_total, D), jnp.bfloat16).at[route_rows].set(token_routes)
    weight_flat = route_weights.reshape(-1)
    grad_routes = jnp.repeat(out_grad.astype(jnp.float32), TOP, axis=0)
    dy_all = jnp.zeros((slot_total, D), jnp.bfloat16).at[route_rows].set((weight_flat[:, None] * grad_routes).astype(jnp.bfloat16))
    y_all, dx_all, gate_up_grad, down_grad = lax.map(expert_pass, (x_all.reshape(EXPERTS, group_total * CAP, D), dy_all.reshape(EXPERTS, group_total * CAP, D), gate_up_weight, down_weight))
    y_routes = y_all.reshape(slot_total, D)[route_rows].astype(jnp.float32)
    layer_out = (weight_flat[:, None] * y_routes).reshape(TOKENS, TOP, D).sum(axis=1).astype(jnp.bfloat16)
    route_grad = jnp.sum(grad_routes * y_routes, axis=1).reshape(TOKENS, TOP)
    dx_routes = dx_all.reshape(slot_total, D)[route_rows].astype(jnp.float32)
    token_grad = dx_routes.reshape(TOKENS, TOP, D).sum(axis=1).astype(jnp.bfloat16)
    return layer_out, token_grad, route_grad, gate_up_grad, down_grad
```

```python
import jax
import jax.numpy as jnp
from jax import lax
from jax.sharding import PartitionSpec as P


def local(tokens, expert_ids, route_weights, gate_up_weight, down_weight, out_grad):
    tok_count, piece_width = tokens.shape
    top_count = expert_ids.shape[1]
    group_count = lax.axis_size("expert")
    local_count = gate_up_weight.shape[0]
    hidden_units = down_weight.shape[1]
    expert_total = local_count * group_count
    capacity = 3 * tok_count * top_count // (2 * expert_total)
    slot_count = expert_total * capacity
    rows_all = group_count * capacity
    route_count = tok_count * top_count
    block_shape = (local_count, group_count, capacity, piece_width)
    route_ids = expert_ids.reshape(-1)
    onehot = (route_ids[:, None] == jnp.arange(expert_total, dtype=jnp.int32)[None, :]).astype(
        jnp.bfloat16
    )
    order = jnp.arange(route_count, dtype=jnp.int32)
    lower = (order[None, :] < order[:, None]).astype(jnp.bfloat16)
    earlier = jnp.dot(lower, onehot, preferred_element_type=jnp.float32)
    slot_rank = jnp.sum(onehot.astype(jnp.float32) * earlier, axis=1).astype(jnp.int32)
    slot_index = (
        route_ids % local_count * rows_all + route_ids // local_count * capacity + slot_rank
    )
    route_hit = slot_index[:, None] == jnp.arange(slot_count, dtype=jnp.int32)[None, :]
    token_hit = jnp.any(route_hit.reshape(tok_count, top_count, slot_count), axis=1).astype(
        jnp.bfloat16
    )
    weight_flat = route_weights.reshape(-1)
    slot_weight = jnp.sum(jnp.where(route_hit, weight_flat[:, None], 0.0), axis=0)
    outbound = lax.dot_general(
        token_hit, tokens, (((0,), (0,)), ((), ())), preferred_element_type=jnp.float32
    ).astype(jnp.bfloat16)
    grad_outbound = (
        slot_weight[:, None]
        * lax.dot_general(
            token_hit, out_grad, (((0,), (0,)), ((), ())), preferred_element_type=jnp.float32
        )
    ).astype(jnp.bfloat16)
    both = jnp.stack([outbound, grad_outbound]).reshape((2,) + block_shape)
    both = lax.all_to_all(both, "expert", split_axis=2, concat_axis=2, tiled=True)
    arrived = both[0].reshape(local_count, rows_all, piece_width)
    grad_arrived = both[1].reshape(local_count, rows_all, piece_width)
    rows = arrived
    preact = lax.psum_scatter(
        jnp.einsum("lrk,lkf->rlf", rows, gate_up_weight, preferred_element_type=jnp.float32).astype(
            jnp.bfloat16
        ),
        "dp",
        scatter_dimension=0,
        tiled=True,
    ).astype(jnp.float32)
    gate_pre = preact[..., :hidden_units]
    up_pre = preact[..., hidden_units:]
    sigmoid_gate = jax.nn.sigmoid(gate_pre)
    activation = gate_pre * sigmoid_gate
    hidden_mine = (activation * up_pre).astype(jnp.bfloat16)
    hidden_all = lax.all_gather(hidden_mine, "dp", axis=0, tiled=True)
    out_slice = jnp.einsum(
        "rlf,lfk->lrk", hidden_all, down_weight, preferred_element_type=jnp.float32
    ).astype(jnp.bfloat16)
    grad_routes = jnp.repeat(out_grad, top_count, axis=0).astype(jnp.float32)
    returned = lax.all_to_all(
        out_slice.reshape(block_shape), "expert", split_axis=1, concat_axis=1, tiled=True
    )
    route_pick = route_hit.astype(jnp.bfloat16)
    y_routes = jnp.dot(
        route_pick, returned.reshape(slot_count, piece_width), preferred_element_type=jnp.float32
    )
    layer_out = (
        (weight_flat[:, None] * y_routes)
        .reshape(tok_count, top_count, piece_width)
        .sum(axis=1)
        .astype(jnp.bfloat16)
    )
    partial_dot = jnp.sum(grad_routes * y_routes, axis=1).reshape(tok_count, top_count)
    route_grad = lax.psum(partial_dot, "dp")
    rows = grad_arrived
    hidden_grad = lax.psum_scatter(
        jnp.einsum("lrk,lfk->rlf", rows, down_weight, preferred_element_type=jnp.float32).astype(
            jnp.bfloat16
        ),
        "dp",
        scatter_dimension=0,
        tiled=True,
    ).astype(jnp.float32)
    gate_grad = hidden_grad * up_pre * sigmoid_gate * (1.0 + gate_pre * (1.0 - sigmoid_gate))
    up_grad = hidden_grad * activation
    preact_grad = jnp.concatenate([gate_grad, up_grad], axis=2).astype(jnp.bfloat16)
    preact_grad_all = lax.all_gather(preact_grad, "dp", axis=0, tiled=True)
    x_grad_slice = jnp.einsum(
        "rlf,lkf->lrk", preact_grad_all, gate_up_weight, preferred_element_type=jnp.float32
    ).astype(jnp.bfloat16)
    gate_up_grad = jnp.einsum(
        "lrk,rlf->lkf", arrived, preact_grad_all, preferred_element_type=jnp.float32
    ).astype(jnp.bfloat16)
    down_grad = jnp.einsum(
        "rlf,lrk->lfk", hidden_all, grad_arrived, preferred_element_type=jnp.float32
    ).astype(jnp.bfloat16)
    grad_back = lax.all_to_all(
        x_grad_slice.reshape(block_shape), "expert", split_axis=1, concat_axis=1, tiled=True
    )
    token_grad = jnp.dot(
        token_hit, grad_back.reshape(slot_count, piece_width), preferred_element_type=jnp.float32
    ).astype(jnp.bfloat16)
    return (layer_out, token_grad, route_grad, gate_up_grad, down_grad)


def solution(mesh):
    placed = (
        P("expert", "dp"),
        P("expert", None),
        P("expert", None),
        P("expert", "dp", None),
        P("expert", None, "dp"),
        P("expert", "dp"),
    )
    return jax.shard_map(
        local,
        mesh=mesh,
        in_specs=placed,
        out_specs=(
            P("expert", "dp"),
            P("expert", "dp"),
            P("expert", None),
            P("expert", "dp", None),
            P("expert", None, "dp"),
        ),
        check_vma=False,
    )
```

```python
import jax
import jax.numpy as jnp
from jax import lax
from jax.sharding import PartitionSpec as P


def local(tokens, expert_ids, route_weights, gate_up_weight, down_weight, out_grad):
    tok_count, piece_width = tokens.shape
    top_count = expert_ids.shape[1]
    group_count = lax.axis_size("expert")
    local_count = gate_up_weight.shape[0]
    hidden_units = down_weight.shape[1]
    expert_total = local_count * group_count
    capacity = 3 * tok_count * top_count // (2 * expert_total)
    slot_count = expert_total * capacity
    rows_all = group_count * capacity
    route_count = tok_count * top_count
    block_shape = (local_count, group_count, capacity, piece_width)
    route_ids = expert_ids.reshape(-1)
    onehot = (route_ids[:, None] == jnp.arange(expert_total, dtype=jnp.int32)[None, :]).astype(
        jnp.bfloat16
    )
    order = jnp.arange(route_count, dtype=jnp.int32)
    lower = (order[None, :] < order[:, None]).astype(jnp.bfloat16)
    earlier = jnp.dot(lower, onehot, preferred_element_type=jnp.float32)
    slot_rank = jnp.sum(onehot.astype(jnp.float32) * earlier, axis=1).astype(jnp.int32)
    slot_index = (
        route_ids % local_count * rows_all + route_ids // local_count * capacity + slot_rank
    )
    route_hit = slot_index[:, None] == jnp.arange(slot_count, dtype=jnp.int32)[None, :]
    token_hit = jnp.any(route_hit.reshape(tok_count, top_count, slot_count), axis=1).astype(
        jnp.bfloat16
    )
    weight_flat = route_weights.reshape(-1)
    slot_weight = jnp.sum(jnp.where(route_hit, weight_flat[:, None], 0.0), axis=0)
    outbound = lax.dot_general(
        token_hit, tokens, (((0,), (0,)), ((), ())), preferred_element_type=jnp.float32
    ).astype(jnp.bfloat16)
    grad_outbound = (
        slot_weight[:, None]
        * lax.dot_general(
            token_hit, out_grad, (((0,), (0,)), ((), ())), preferred_element_type=jnp.float32
        )
    ).astype(jnp.bfloat16)
    both = jnp.stack([outbound, grad_outbound]).reshape((2,) + block_shape)
    both = lax.all_to_all(both, "expert", split_axis=2, concat_axis=2, tiled=True)
    arrived = both[0].reshape(local_count, rows_all, piece_width)
    grad_arrived = both[1].reshape(local_count, rows_all, piece_width)
    gate_up_part = jnp.einsum(
        "lrk,lkf->rlf", arrived, gate_up_weight, preferred_element_type=jnp.float32
    ).astype(jnp.bfloat16)
    hidden_grad_part = jnp.einsum(
        "lrk,lfk->rlf", grad_arrived, down_weight, preferred_element_type=jnp.float32
    ).astype(jnp.bfloat16)
    summed = lax.psum_scatter(
        jnp.concatenate([gate_up_part, hidden_grad_part], axis=2),
        "dp",
        scatter_dimension=0,
        tiled=True,
    ).astype(jnp.float32)
    gate_pre = summed[..., :hidden_units]
    up_pre = summed[..., hidden_units : 2 * hidden_units]
    hidden_grad = summed[..., 2 * hidden_units :]
    sigmoid_gate = jax.nn.sigmoid(gate_pre)
    activation = gate_pre * sigmoid_gate
    hidden_mine = (activation * up_pre).astype(jnp.bfloat16)
    gate_grad = hidden_grad * up_pre * sigmoid_gate * (1.0 + gate_pre * (1.0 - sigmoid_gate))
    up_grad = hidden_grad * activation
    preact_grad = jnp.concatenate([gate_grad, up_grad], axis=2).astype(jnp.bfloat16)
    gathered = lax.all_gather(
        jnp.concatenate([hidden_mine, preact_grad], axis=2), "dp", axis=0, tiled=True
    )
    hidden_all = gathered[..., :hidden_units]
    preact_grad_all = gathered[..., hidden_units:]
    out_slice = jnp.einsum(
        "rlf,lfk->lrk", hidden_all, down_weight, preferred_element_type=jnp.float32
    ).astype(jnp.bfloat16)
    grad_routes = jnp.repeat(out_grad, top_count, axis=0).astype(jnp.float32)
    returned = lax.all_to_all(
        out_slice.reshape(block_shape), "expert", split_axis=1, concat_axis=1, tiled=True
    )
    route_pick = route_hit.astype(jnp.bfloat16)
    y_routes = jnp.dot(
        route_pick, returned.reshape(slot_count, piece_width), preferred_element_type=jnp.float32
    )
    layer_out = (
        (weight_flat[:, None] * y_routes)
        .reshape(tok_count, top_count, piece_width)
        .sum(axis=1)
        .astype(jnp.bfloat16)
    )
    partial_dot = jnp.sum(grad_routes * y_routes, axis=1).reshape(tok_count, top_count)
    route_grad = lax.psum(partial_dot, "dp")
    x_grad_slice = jnp.einsum(
        "rlf,lkf->lrk", preact_grad_all, gate_up_weight, preferred_element_type=jnp.float32
    ).astype(jnp.bfloat16)
    gate_up_grad = jnp.einsum(
        "lrk,rlf->lkf", arrived, preact_grad_all, preferred_element_type=jnp.float32
    ).astype(jnp.bfloat16)
    down_grad = jnp.einsum(
        "rlf,lrk->lfk", hidden_all, grad_arrived, preferred_element_type=jnp.float32
    ).astype(jnp.bfloat16)
    grad_back = lax.all_to_all(
        x_grad_slice.reshape(block_shape), "expert", split_axis=1, concat_axis=1, tiled=True
    )
    token_grad = jnp.dot(
        token_hit, grad_back.reshape(slot_count, piece_width), preferred_element_type=jnp.float32
    ).astype(jnp.bfloat16)
    return (layer_out, token_grad, route_grad, gate_up_grad, down_grad)


def solution(mesh):
    placed = (
        P("expert", "dp"),
        P("expert", None),
        P("expert", None),
        P("expert", "dp", None),
        P("expert", None, "dp"),
        P("expert", "dp"),
    )
    return jax.shard_map(
        local,
        mesh=mesh,
        in_specs=placed,
        out_specs=(
            P("expert", "dp"),
            P("expert", "dp"),
            P("expert", None),
            P("expert", "dp", None),
            P("expert", None, "dp"),
        ),
        check_vma=False,
    )
```

```python
import jax
import jax.numpy as jnp
from jax import lax
from jax.sharding import PartitionSpec as P


def local(tokens, expert_ids, route_weights, gate_up_weight, down_weight, out_grad):
    tok_count, piece_width = tokens.shape
    top_count = expert_ids.shape[1]
    group_count = lax.axis_size("expert")
    local_count = gate_up_weight.shape[0]
    hidden_units = down_weight.shape[1]
    expert_total = local_count * group_count
    capacity = 3 * tok_count * top_count // (2 * expert_total)
    slot_count = expert_total * capacity
    rows_all = group_count * capacity
    route_count = tok_count * top_count
    block_shape = (local_count, group_count, capacity, piece_width)
    route_ids = expert_ids.reshape(-1)
    onehot = (route_ids[:, None] == jnp.arange(expert_total, dtype=jnp.int32)[None, :]).astype(
        jnp.bfloat16
    )
    order = jnp.arange(route_count, dtype=jnp.int32)
    lower = (order[None, :] < order[:, None]).astype(jnp.bfloat16)
    earlier = jnp.dot(lower, onehot, preferred_element_type=jnp.float32)
    slot_rank = jnp.sum(onehot.astype(jnp.float32) * earlier, axis=1).astype(jnp.int32)
    slot_index = (
        route_ids % local_count * rows_all + route_ids // local_count * capacity + slot_rank
    )
    route_hit = slot_index[:, None] == jnp.arange(slot_count, dtype=jnp.int32)[None, :]
    token_hit = jnp.any(route_hit.reshape(tok_count, top_count, slot_count), axis=1).astype(
        jnp.bfloat16
    )
    weight_flat = route_weights.reshape(-1)
    slot_weight = jnp.sum(jnp.where(route_hit, weight_flat[:, None], 0.0), axis=0)
    outbound = lax.dot_general(
        token_hit, tokens, (((0,), (0,)), ((), ())), preferred_element_type=jnp.float32
    ).astype(jnp.bfloat16)
    grad_outbound = (
        slot_weight[:, None]
        * lax.dot_general(
            token_hit, out_grad, (((0,), (0,)), ((), ())), preferred_element_type=jnp.float32
        )
    ).astype(jnp.bfloat16)
    both = jnp.stack([outbound, grad_outbound]).reshape((2,) + block_shape)
    both = lax.all_to_all(both, "expert", split_axis=2, concat_axis=2, tiled=True)
    arrived = both[0].reshape(local_count, rows_all, piece_width)
    grad_arrived = both[1].reshape(local_count, rows_all, piece_width)
    gate_up_part = jnp.einsum(
        "lrk,lkf->rlf", arrived, gate_up_weight, preferred_element_type=jnp.float32
    ).astype(jnp.bfloat16)
    hidden_grad_part = jnp.einsum(
        "lrk,lfk->rlf", grad_arrived, down_weight, preferred_element_type=jnp.float32
    ).astype(jnp.bfloat16)
    summed = lax.psum_scatter(
        jnp.concatenate([gate_up_part, hidden_grad_part], axis=2),
        "dp",
        scatter_dimension=0,
        tiled=True,
    ).astype(jnp.float32)
    gate_pre = summed[..., :hidden_units]
    up_pre = summed[..., hidden_units : 2 * hidden_units]
    hidden_grad = summed[..., 2 * hidden_units :]
    sigmoid_gate = jax.nn.sigmoid(gate_pre)
    activation = gate_pre * sigmoid_gate
    hidden_mine = (activation * up_pre).astype(jnp.bfloat16)
    gate_grad = hidden_grad * up_pre * sigmoid_gate * (1.0 + gate_pre * (1.0 - sigmoid_gate))
    up_grad = hidden_grad * activation
    preact_grad = jnp.concatenate([gate_grad, up_grad], axis=2).astype(jnp.bfloat16)
    hidden_all = lax.all_gather(hidden_mine, "dp", axis=0, tiled=True)
    preact_grad_all = lax.all_gather(preact_grad, "dp", axis=0, tiled=True)
    out_slice = jnp.einsum(
        "rlf,lfk->lrk", hidden_all, down_weight, preferred_element_type=jnp.float32
    ).astype(jnp.bfloat16)
    grad_routes = jnp.repeat(out_grad, top_count, axis=0).astype(jnp.float32)
    returned = lax.all_to_all(
        out_slice.reshape(block_shape), "expert", split_axis=1, concat_axis=1, tiled=True
    )
    route_pick = route_hit.astype(jnp.bfloat16)
    y_routes = jnp.dot(
        route_pick, returned.reshape(slot_count, piece_width), preferred_element_type=jnp.float32
    )
    layer_out = (
        (weight_flat[:, None] * y_routes)
        .reshape(tok_count, top_count, piece_width)
        .sum(axis=1)
        .astype(jnp.bfloat16)
    )
    partial_dot = jnp.sum(grad_routes * y_routes, axis=1).reshape(tok_count, top_count)
    route_grad = lax.psum(partial_dot, "dp")
    x_grad_slice = jnp.einsum(
        "rlf,lkf->lrk", preact_grad_all, gate_up_weight, preferred_element_type=jnp.float32
    ).astype(jnp.bfloat16)
    gate_up_grad = jnp.einsum(
        "lrk,rlf->lkf", arrived, preact_grad_all, preferred_element_type=jnp.float32
    ).astype(jnp.bfloat16)
    down_grad = jnp.einsum(
        "rlf,lrk->lfk", hidden_all, grad_arrived, preferred_element_type=jnp.float32
    ).astype(jnp.bfloat16)
    grad_back = lax.all_to_all(
        x_grad_slice.reshape(block_shape), "expert", split_axis=1, concat_axis=1, tiled=True
    )
    token_grad = jnp.dot(
        token_hit, grad_back.reshape(slot_count, piece_width), preferred_element_type=jnp.float32
    ).astype(jnp.bfloat16)
    return (layer_out, token_grad, route_grad, gate_up_grad, down_grad)


def solution(mesh):
    placed = (
        P("expert", "dp"),
        P("expert", None),
        P("expert", None),
        P("expert", "dp", None),
        P("expert", None, "dp"),
        P("expert", "dp"),
    )
    return jax.shard_map(
        local,
        mesh=mesh,
        in_specs=placed,
        out_specs=(
            P("expert", "dp"),
            P("expert", "dp"),
            P("expert", None),
            P("expert", "dp", None),
            P("expert", None, "dp"),
        ),
        check_vma=False,
    )
```

```python
import jax
import jax.numpy as jnp
from jax import lax
from jax.sharding import PartitionSpec as P


def layer(tokens, expert_ids, route_weights, gate_up_weight, down_weight, out_grad):
    tok_count, piece_width = tokens.shape
    top_count = expert_ids.shape[1]
    group_count = lax.axis_size("expert")
    local_count = gate_up_weight.shape[0]
    hidden_units = down_weight.shape[1]
    expert_total = local_count * group_count
    capacity = 3 * tok_count * top_count // (2 * expert_total)
    slot_count = expert_total * capacity
    rows_all = group_count * capacity
    route_count = tok_count * top_count
    block_shape = (local_count, group_count, capacity, piece_width)
    route_ids = expert_ids.reshape(-1)
    onehot = (route_ids[:, None] == jnp.arange(expert_total, dtype=jnp.int32)[None, :]).astype(
        jnp.bfloat16
    )
    order = jnp.arange(route_count, dtype=jnp.int32)
    lower = (order[None, :] < order[:, None]).astype(jnp.bfloat16)
    earlier = jnp.dot(lower, onehot, preferred_element_type=jnp.float32)
    slot_rank = jnp.sum(onehot.astype(jnp.float32) * earlier, axis=1).astype(jnp.int32)
    slot_index = (
        route_ids % local_count * rows_all + route_ids // local_count * capacity + slot_rank
    )
    route_hit = slot_index[:, None] == jnp.arange(slot_count, dtype=jnp.int32)[None, :]
    token_hit = jnp.any(route_hit.reshape(tok_count, top_count, slot_count), axis=1).astype(
        jnp.bfloat16
    )
    weight_flat = route_weights.reshape(-1)
    slot_weight = jnp.sum(jnp.where(route_hit, weight_flat[:, None], 0.0), axis=0)
    outbound = lax.dot_general(
        token_hit, tokens, (((0,), (0,)), ((), ())), preferred_element_type=jnp.float32
    ).astype(jnp.bfloat16)
    grad_outbound = (
        slot_weight[:, None]
        * lax.dot_general(
            token_hit, out_grad, (((0,), (0,)), ((), ())), preferred_element_type=jnp.float32
        )
    ).astype(jnp.bfloat16)
    arrived = lax.all_to_all(
        outbound.reshape(block_shape), "expert", split_axis=1, concat_axis=1, tiled=True
    ).reshape(local_count, rows_all, piece_width)
    preact = lax.psum_scatter(
        jnp.einsum(
            "lrk,lkf->rlf", arrived, gate_up_weight, preferred_element_type=jnp.float32
        ).astype(jnp.bfloat16),
        "dp",
        scatter_dimension=0,
        tiled=True,
    ).astype(jnp.float32)
    grad_arrived = lax.all_to_all(
        grad_outbound.reshape(block_shape), "expert", split_axis=1, concat_axis=1, tiled=True
    ).reshape(local_count, rows_all, piece_width)
    preact, grad_arrived = lax.optimization_barrier((preact, grad_arrived))
    gate_pre = preact[..., :hidden_units]
    up_pre = preact[..., hidden_units:]
    sigmoid_gate = jax.nn.sigmoid(gate_pre)
    activation = gate_pre * sigmoid_gate
    hidden_mine = (activation * up_pre).astype(jnp.bfloat16)
    hidden_mine, grad_arrived = lax.optimization_barrier((hidden_mine, grad_arrived))
    hidden_all = lax.all_gather(hidden_mine, "dp", axis=0, tiled=True)
    hidden_grad_part = jnp.einsum(
        "lrk,lfk->rlf", grad_arrived, down_weight, preferred_element_type=jnp.float32
    ).astype(jnp.bfloat16)
    hidden_grad = lax.psum_scatter(hidden_grad_part, "dp", scatter_dimension=0, tiled=True)
    hidden_all, _ = lax.optimization_barrier((hidden_all, hidden_grad_part))
    out_slice = jnp.einsum(
        "rlf,lfk->lrk", hidden_all, down_weight, preferred_element_type=jnp.float32
    ).astype(jnp.bfloat16)
    hidden_grad = hidden_grad.astype(jnp.float32)
    gate_grad = hidden_grad * up_pre * sigmoid_gate * (1.0 + gate_pre * (1.0 - sigmoid_gate))
    up_grad = hidden_grad * activation
    preact_grad = jnp.concatenate([gate_grad, up_grad], axis=2).astype(jnp.bfloat16)
    grad_routes = jnp.repeat(out_grad, top_count, axis=0).astype(jnp.float32)
    returned = lax.all_to_all(
        out_slice.reshape(block_shape), "expert", split_axis=1, concat_axis=1, tiled=True
    )
    route_pick = route_hit.astype(jnp.bfloat16)
    y_routes = jnp.dot(
        route_pick, returned.reshape(slot_count, piece_width), preferred_element_type=jnp.float32
    )
    layer_out = (
        (weight_flat[:, None] * y_routes)
        .reshape(tok_count, top_count, piece_width)
        .sum(axis=1)
        .astype(jnp.bfloat16)
    )
    partial_dot = jnp.sum(grad_routes * y_routes, axis=1).reshape(tok_count, top_count)
    route_grad = lax.psum(partial_dot, "dp")
    down_grad = jnp.einsum(
        "rlf,lrk->lfk", hidden_all, grad_arrived, preferred_element_type=jnp.float32
    ).astype(jnp.bfloat16)
    token_grad = jnp.zeros((tok_count, piece_width), jnp.float32)
    gate_up_grads = []
    for l in range(local_count):
        preact_grad_all = lax.all_gather(preact_grad[:, l], "dp", axis=0, tiled=True)
        x_grad_slice = lax.dot_general(
            preact_grad_all,
            gate_up_weight[l],
            (((1,), (1,)), ((), ())),
            preferred_element_type=jnp.float32,
        ).astype(jnp.bfloat16)
        gate_up_grads.append(
            lax.dot_general(
                arrived[l],
                preact_grad_all,
                (((0,), (0,)), ((), ())),
                preferred_element_type=jnp.float32,
            ).astype(jnp.bfloat16)
        )
        grad_back = lax.all_to_all(
            x_grad_slice.reshape(group_count, capacity, piece_width),
            "expert",
            split_axis=0,
            concat_axis=0,
            tiled=True,
        )
        token_grad = token_grad + jnp.dot(
            token_hit[:, l * rows_all : (l + 1) * rows_all],
            grad_back.reshape(rows_all, piece_width),
            preferred_element_type=jnp.float32,
        )
    token_grad = token_grad.astype(jnp.bfloat16)
    gate_up_grad = jnp.stack(gate_up_grads)
    return (layer_out, token_grad, route_grad, gate_up_grad, down_grad)


def solution(mesh):
    placed = (
        P("expert", "dp"),
        P("expert", None),
        P("expert", None),
        P("expert", "dp", None),
        P("expert", None, "dp"),
        P("expert", "dp"),
    )
    return jax.shard_map(
        layer,
        mesh=mesh,
        in_specs=placed,
        out_specs=(
            P("expert", "dp"),
            P("expert", "dp"),
            P("expert", None),
            P("expert", "dp", None),
            P("expert", None, "dp"),
        ),
        check_vma=False,
    )
```

```python
import jax
import jax.numpy as jnp
from jax import lax
from jax.sharding import PartitionSpec as P


def layer(tokens, expert_ids, route_weights, gate_up_weight, down_weight, out_grad):
    tok_count, piece_width = tokens.shape
    top_count = expert_ids.shape[1]
    group_count = lax.axis_size("expert")
    local_count = gate_up_weight.shape[0]
    hidden_units = down_weight.shape[1]
    expert_total = local_count * group_count
    capacity = 3 * tok_count * top_count // (2 * expert_total)
    slot_count = expert_total * capacity
    rows_all = group_count * capacity
    route_count = tok_count * top_count
    block_shape = (local_count, group_count, capacity, piece_width)
    route_ids = expert_ids.reshape(-1)
    onehot = (route_ids[:, None] == jnp.arange(expert_total, dtype=jnp.int32)[None, :]).astype(
        jnp.bfloat16
    )
    order = jnp.arange(route_count, dtype=jnp.int32)
    lower = (order[None, :] < order[:, None]).astype(jnp.bfloat16)
    earlier = jnp.dot(lower, onehot, preferred_element_type=jnp.float32)
    slot_rank = jnp.sum(onehot.astype(jnp.float32) * earlier, axis=1).astype(jnp.int32)
    slot_index = (
        route_ids % local_count * rows_all + route_ids // local_count * capacity + slot_rank
    )
    route_hit = slot_index[:, None] == jnp.arange(slot_count, dtype=jnp.int32)[None, :]
    token_hit = jnp.any(route_hit.reshape(tok_count, top_count, slot_count), axis=1).astype(
        jnp.bfloat16
    )
    weight_flat = route_weights.reshape(-1)
    slot_weight = jnp.sum(jnp.where(route_hit, weight_flat[:, None], 0.0), axis=0)
    outbound = lax.dot_general(
        token_hit, tokens, (((0,), (0,)), ((), ())), preferred_element_type=jnp.float32
    ).astype(jnp.bfloat16)
    grad_outbound = (
        slot_weight[:, None]
        * lax.dot_general(
            token_hit, out_grad, (((0,), (0,)), ((), ())), preferred_element_type=jnp.float32
        )
    ).astype(jnp.bfloat16)
    arrived = lax.all_to_all(
        outbound.reshape(block_shape), "expert", split_axis=1, concat_axis=1, tiled=True
    ).reshape(local_count, rows_all, piece_width)
    preact = lax.psum(
        jnp.einsum(
            "lrk,lkf->rlf", arrived, gate_up_weight, preferred_element_type=jnp.float32
        ).astype(jnp.bfloat16),
        "dp",
    ).astype(jnp.float32)
    grad_arrived = lax.all_to_all(
        grad_outbound.reshape(block_shape), "expert", split_axis=1, concat_axis=1, tiled=True
    ).reshape(local_count, rows_all, piece_width)
    preact, grad_arrived = lax.optimization_barrier((preact, grad_arrived))
    gate_pre = preact[..., :hidden_units]
    up_pre = preact[..., hidden_units:]
    sigmoid_gate = jax.nn.sigmoid(gate_pre)
    activation = gate_pre * sigmoid_gate
    hidden_all = (activation * up_pre).astype(jnp.bfloat16)
    out_slice = jnp.einsum(
        "rlf,lfk->lrk", hidden_all, down_weight, preferred_element_type=jnp.float32
    ).astype(jnp.bfloat16)
    out_slice, grad_arrived = lax.optimization_barrier((out_slice, grad_arrived))
    hidden_grad_part = jnp.einsum(
        "lrk,lfk->rlf", grad_arrived, down_weight, preferred_element_type=jnp.float32
    ).astype(jnp.bfloat16)
    hidden_grad = lax.psum(hidden_grad_part, "dp")
    hidden_grad = hidden_grad.astype(jnp.float32)
    gate_grad = hidden_grad * up_pre * sigmoid_gate * (1.0 + gate_pre * (1.0 - sigmoid_gate))
    up_grad = hidden_grad * activation
    preact_grad_all = jnp.concatenate([gate_grad, up_grad], axis=2).astype(jnp.bfloat16)
    grad_routes = jnp.repeat(out_grad, top_count, axis=0).astype(jnp.float32)
    returned = lax.all_to_all(
        out_slice.reshape(block_shape), "expert", split_axis=1, concat_axis=1, tiled=True
    )
    route_pick = route_hit.astype(jnp.bfloat16)
    y_routes = jnp.dot(
        route_pick, returned.reshape(slot_count, piece_width), preferred_element_type=jnp.float32
    )
    layer_out = (
        (weight_flat[:, None] * y_routes)
        .reshape(tok_count, top_count, piece_width)
        .sum(axis=1)
        .astype(jnp.bfloat16)
    )
    partial_dot = jnp.sum(grad_routes * y_routes, axis=1).reshape(tok_count, top_count)
    route_grad = lax.psum(partial_dot, "dp")
    x_grad_slice = jnp.einsum(
        "rlf,lkf->lrk", preact_grad_all, gate_up_weight, preferred_element_type=jnp.float32
    ).astype(jnp.bfloat16)
    gate_up_grad = jnp.einsum(
        "lrk,rlf->lkf", arrived, preact_grad_all, preferred_element_type=jnp.float32
    ).astype(jnp.bfloat16)
    down_grad = jnp.einsum(
        "rlf,lrk->lfk", hidden_all, grad_arrived, preferred_element_type=jnp.float32
    ).astype(jnp.bfloat16)
    grad_back = lax.all_to_all(
        x_grad_slice.reshape(block_shape), "expert", split_axis=1, concat_axis=1, tiled=True
    )
    token_grad = jnp.dot(
        token_hit, grad_back.reshape(slot_count, piece_width), preferred_element_type=jnp.float32
    ).astype(jnp.bfloat16)
    return (layer_out, token_grad, route_grad, gate_up_grad, down_grad)


def solution(mesh):
    placed = (
        P("expert", "dp"),
        P("expert", None),
        P("expert", None),
        P("expert", "dp", None),
        P("expert", None, "dp"),
        P("expert", "dp"),
    )
    return jax.shard_map(
        layer,
        mesh=mesh,
        in_specs=placed,
        out_specs=(
            P("expert", "dp"),
            P("expert", "dp"),
            P("expert", None),
            P("expert", "dp", None),
            P("expert", None, "dp"),
        ),
        check_vma=False,
    )
```

```python
import jax
import jax.numpy as jnp
from jax import lax
from jax.sharding import PartitionSpec as P


def layer(tokens, expert_ids, route_weights, gate_up_weight, down_weight, out_grad):
    tok_count, piece_width = tokens.shape
    top_count = expert_ids.shape[1]
    group_count = lax.axis_size("expert")
    local_count = gate_up_weight.shape[0]
    hidden_units = down_weight.shape[1]
    expert_total = local_count * group_count
    capacity = 3 * tok_count * top_count // (2 * expert_total)
    slot_count = expert_total * capacity
    rows_all = group_count * capacity
    route_count = tok_count * top_count
    block_shape = (local_count, group_count, capacity, piece_width)
    route_ids = expert_ids.reshape(-1)
    onehot = (route_ids[:, None] == jnp.arange(expert_total, dtype=jnp.int32)[None, :]).astype(
        jnp.bfloat16
    )
    order = jnp.arange(route_count, dtype=jnp.int32)
    lower = (order[None, :] < order[:, None]).astype(jnp.bfloat16)
    earlier = jnp.dot(lower, onehot, preferred_element_type=jnp.float32)
    slot_rank = jnp.sum(onehot.astype(jnp.float32) * earlier, axis=1).astype(jnp.int32)
    slot_index = (
        route_ids % local_count * rows_all + route_ids // local_count * capacity + slot_rank
    )
    route_hit = slot_index[:, None] == jnp.arange(slot_count, dtype=jnp.int32)[None, :]
    token_hit = jnp.any(route_hit.reshape(tok_count, top_count, slot_count), axis=1).astype(
        jnp.bfloat16
    )
    weight_flat = route_weights.reshape(-1)
    slot_weight = jnp.sum(jnp.where(route_hit, weight_flat[:, None], 0.0), axis=0)
    outbound = lax.dot_general(
        token_hit, tokens, (((0,), (0,)), ((), ())), preferred_element_type=jnp.float32
    ).astype(jnp.bfloat16)
    grad_outbound = (
        slot_weight[:, None]
        * lax.dot_general(
            token_hit, out_grad, (((0,), (0,)), ((), ())), preferred_element_type=jnp.float32
        )
    ).astype(jnp.bfloat16)
    arrived = lax.all_to_all(
        outbound.reshape(block_shape), "expert", split_axis=1, concat_axis=1, tiled=True
    ).reshape(local_count, rows_all, piece_width)
    preact = lax.psum_scatter(
        jnp.einsum(
            "lrk,lkf->rlf", arrived, gate_up_weight, preferred_element_type=jnp.float32
        ).astype(jnp.bfloat16),
        "dp",
        scatter_dimension=0,
        tiled=True,
    ).astype(jnp.float32)
    grad_arrived = lax.all_to_all(
        grad_outbound.reshape(block_shape), "expert", split_axis=1, concat_axis=1, tiled=True
    ).reshape(local_count, rows_all, piece_width)
    preact, grad_arrived = lax.optimization_barrier((preact, grad_arrived))
    gate_pre = preact[..., :hidden_units]
    up_pre = preact[..., hidden_units:]
    sigmoid_gate = jax.nn.sigmoid(gate_pre)
    activation = gate_pre * sigmoid_gate
    hidden_mine = (activation * up_pre).astype(jnp.bfloat16)
    hidden_mine, grad_arrived = lax.optimization_barrier((hidden_mine, grad_arrived))
    hidden_all = lax.all_gather(hidden_mine, "dp", axis=0, tiled=True)
    hidden_grad_part = jnp.einsum(
        "lrk,lfk->rlf", grad_arrived, down_weight, preferred_element_type=jnp.float32
    ).astype(jnp.bfloat16)
    hidden_grad = lax.psum_scatter(hidden_grad_part, "dp", scatter_dimension=0, tiled=True)
    hidden_all, _ = lax.optimization_barrier((hidden_all, hidden_grad_part))
    out_slice = jnp.einsum(
        "rlf,lfk->lrk", hidden_all, down_weight, preferred_element_type=jnp.float32
    ).astype(jnp.bfloat16)
    hidden_grad = hidden_grad.astype(jnp.float32)
    gate_grad = hidden_grad * up_pre * sigmoid_gate * (1.0 + gate_pre * (1.0 - sigmoid_gate))
    up_grad = hidden_grad * activation
    preact_grad = jnp.concatenate([gate_grad, up_grad], axis=2).astype(jnp.bfloat16)
    preact_grad_all = lax.all_gather(preact_grad, "dp", axis=0, tiled=True)
    grad_routes = jnp.repeat(out_grad, top_count, axis=0).astype(jnp.float32)
    returned = lax.all_to_all(
        out_slice.reshape(block_shape), "expert", split_axis=1, concat_axis=1, tiled=True
    )
    route_pick = route_hit.astype(jnp.bfloat16)
    y_routes = jnp.dot(
        route_pick, returned.reshape(slot_count, piece_width), preferred_element_type=jnp.float32
    )
    layer_out = (
        (weight_flat[:, None] * y_routes)
        .reshape(tok_count, top_count, piece_width)
        .sum(axis=1)
        .astype(jnp.bfloat16)
    )
    partial_dot = jnp.sum(grad_routes * y_routes, axis=1).reshape(tok_count, top_count)
    route_grad = lax.psum(partial_dot, "dp")
    x_grad_slice = jnp.einsum(
        "rlf,lkf->lrk", preact_grad_all, gate_up_weight, preferred_element_type=jnp.float32
    ).astype(jnp.bfloat16)
    gate_up_grad = jnp.einsum(
        "lrk,rlf->lkf", arrived, preact_grad_all, preferred_element_type=jnp.float32
    ).astype(jnp.bfloat16)
    down_grad = jnp.einsum(
        "rlf,lrk->lfk", hidden_all, grad_arrived, preferred_element_type=jnp.float32
    ).astype(jnp.bfloat16)
    grad_back = lax.all_to_all(
        x_grad_slice.reshape(block_shape), "expert", split_axis=1, concat_axis=1, tiled=True
    )
    token_grad = jnp.dot(
        token_hit, grad_back.reshape(slot_count, piece_width), preferred_element_type=jnp.float32
    ).astype(jnp.bfloat16)
    return (layer_out, token_grad, route_grad, gate_up_grad, down_grad)


def solution(mesh):
    placed = (
        P("expert", "dp"),
        P("expert", None),
        P("expert", None),
        P("expert", "dp", None),
        P("expert", None, "dp"),
        P("expert", "dp"),
    )
    return jax.shard_map(
        layer,
        mesh=mesh,
        in_specs=placed,
        out_specs=(
            P("expert", "dp"),
            P("expert", "dp"),
            P("expert", None),
            P("expert", "dp", None),
            P("expert", None, "dp"),
        ),
        check_vma=False,
    )
```

```python
import jax
import jax.numpy as jnp
from jax import lax
from jax.sharding import PartitionSpec as P


def layer(tokens, expert_ids, route_weights, gate_up_weight, down_weight, out_grad):
    tok_count, piece_width = tokens.shape
    top_count = expert_ids.shape[1]
    group_count = lax.axis_size("expert")
    local_count = gate_up_weight.shape[0]
    hidden_units = down_weight.shape[1]
    expert_total = local_count * group_count
    capacity = 3 * tok_count * top_count // (2 * expert_total)
    slot_count = expert_total * capacity
    rows_all = group_count * capacity
    route_count = tok_count * top_count
    block_shape = (local_count, group_count, capacity, piece_width)
    route_ids = expert_ids.reshape(-1)
    onehot = (route_ids[:, None] == jnp.arange(expert_total, dtype=jnp.int32)[None, :]).astype(
        jnp.bfloat16
    )
    order = jnp.arange(route_count, dtype=jnp.int32)
    lower = (order[None, :] < order[:, None]).astype(jnp.bfloat16)
    earlier = jnp.dot(lower, onehot, preferred_element_type=jnp.float32)
    slot_rank = jnp.sum(onehot.astype(jnp.float32) * earlier, axis=1).astype(jnp.int32)
    slot_index = (
        route_ids % local_count * rows_all + route_ids // local_count * capacity + slot_rank
    )
    route_hit = slot_index[:, None] == jnp.arange(slot_count, dtype=jnp.int32)[None, :]
    token_hit = jnp.any(route_hit.reshape(tok_count, top_count, slot_count), axis=1).astype(
        jnp.bfloat16
    )
    weight_flat = route_weights.reshape(-1)
    slot_weight = jnp.sum(jnp.where(route_hit, weight_flat[:, None], 0.0), axis=0)
    outbound = lax.dot_general(
        token_hit, tokens, (((0,), (0,)), ((), ())), preferred_element_type=jnp.float32
    ).astype(jnp.bfloat16)
    grad_outbound = (
        slot_weight[:, None]
        * lax.dot_general(
            token_hit, out_grad, (((0,), (0,)), ((), ())), preferred_element_type=jnp.float32
        )
    ).astype(jnp.bfloat16)
    arrived = lax.all_to_all(
        outbound.reshape(block_shape), "expert", split_axis=1, concat_axis=1, tiled=True
    ).reshape(local_count, rows_all, piece_width)
    preact = lax.psum_scatter(
        jnp.einsum(
            "lrk,lkf->rlf", arrived, gate_up_weight, preferred_element_type=jnp.float32
        ).astype(jnp.bfloat16),
        "dp",
        scatter_dimension=0,
        tiled=True,
    ).astype(jnp.float32)
    grad_arrived = lax.all_to_all(
        grad_outbound.reshape(block_shape), "expert", split_axis=1, concat_axis=1, tiled=True
    ).reshape(local_count, rows_all, piece_width)
    preact, grad_arrived = lax.optimization_barrier((preact, grad_arrived))
    gate_pre = preact[..., :hidden_units]
    up_pre = preact[..., hidden_units:]
    sigmoid_gate = jax.nn.sigmoid(gate_pre)
    activation = gate_pre * sigmoid_gate
    hidden_mine = (activation * up_pre).astype(jnp.bfloat16)
    hidden_mine, grad_arrived = lax.optimization_barrier((hidden_mine, grad_arrived))
    hidden_all = lax.all_gather(hidden_mine, "dp", axis=0, tiled=True)
    hidden_grad_part = jnp.einsum(
        "lrk,lfk->rlf", grad_arrived, down_weight, preferred_element_type=jnp.float32
    ).astype(jnp.bfloat16)
    hidden_grad = lax.psum_scatter(hidden_grad_part, "dp", scatter_dimension=0, tiled=True)
    hidden_all, _ = lax.optimization_barrier((hidden_all, hidden_grad_part))
    out_slice = jnp.einsum(
        "rlf,lfk->lrk", hidden_all, down_weight, preferred_element_type=jnp.float32
    ).astype(jnp.bfloat16)
    hidden_grad = hidden_grad.astype(jnp.float32)
    gate_grad = hidden_grad * up_pre * sigmoid_gate * (1.0 + gate_pre * (1.0 - sigmoid_gate))
    up_grad = hidden_grad * activation
    preact_grad = jnp.concatenate([gate_grad, up_grad], axis=2).astype(jnp.bfloat16)
    preact_grad_all = lax.all_gather(preact_grad, "dp", axis=0, tiled=True)
    grad_routes = jnp.repeat(out_grad, top_count, axis=0).astype(jnp.float32)
    returned = lax.all_to_all(
        out_slice.reshape(block_shape), "expert", split_axis=1, concat_axis=1, tiled=True
    )
    route_pick = route_hit.astype(jnp.bfloat16)
    y_routes = jnp.dot(
        route_pick, returned.reshape(slot_count, piece_width), preferred_element_type=jnp.float32
    )
    layer_out = (
        (weight_flat[:, None] * y_routes)
        .reshape(tok_count, top_count, piece_width)
        .sum(axis=1)
        .astype(jnp.bfloat16)
    )
    partial_dot = jnp.sum(grad_routes * y_routes, axis=1).reshape(tok_count, top_count)
    route_grad = lax.psum(partial_dot, "dp")
    x_grad_slice = jnp.einsum(
        "gclf,lkf->glck",
        preact_grad_all.reshape(group_count, capacity, local_count, 2 * hidden_units),
        gate_up_weight,
        preferred_element_type=jnp.float32,
    ).astype(jnp.bfloat16)
    gate_up_grad = jnp.einsum(
        "lrk,rlf->lkf", arrived, preact_grad_all, preferred_element_type=jnp.float32
    ).astype(jnp.bfloat16)
    down_grad = jnp.einsum(
        "rlf,lrk->lfk", hidden_all, grad_arrived, preferred_element_type=jnp.float32
    ).astype(jnp.bfloat16)
    grad_back = lax.all_to_all(x_grad_slice, "expert", split_axis=0, concat_axis=0, tiled=True)
    token_hit_back = (
        token_hit.reshape(tok_count, local_count, group_count, capacity)
        .transpose(0, 2, 1, 3)
        .reshape(tok_count, slot_count)
    )
    token_grad = jnp.dot(
        token_hit_back, grad_back.reshape(slot_count, piece_width), preferred_element_type=jnp.float32
    ).astype(jnp.bfloat16)
    return (layer_out, token_grad, route_grad, gate_up_grad, down_grad)


def solution(mesh):
    placed = (
        P("expert", "dp"),
        P("expert", None),
        P("expert", None),
        P("expert", "dp", None),
        P("expert", None, "dp"),
        P("expert", "dp"),
    )
    return jax.shard_map(
        layer,
        mesh=mesh,
        in_specs=placed,
        out_specs=(
            P("expert", "dp"),
            P("expert", "dp"),
            P("expert", None),
            P("expert", "dp", None),
            P("expert", None, "dp"),
        ),
        check_vma=False,
    )
```

```python
import jax
import jax.numpy as jnp
from jax import lax
from jax.sharding import PartitionSpec as P


def layer(tokens, expert_ids, route_weights, gate_up_weight, down_weight, out_grad):
    tok_count, piece_width = tokens.shape
    top_count = expert_ids.shape[1]
    group_count = lax.axis_size("expert")
    local_count = gate_up_weight.shape[0]
    hidden_units = down_weight.shape[1]
    expert_total = local_count * group_count
    capacity = 3 * tok_count * top_count // (2 * expert_total)
    slot_count = expert_total * capacity
    rows_all = group_count * capacity
    route_count = tok_count * top_count
    block_shape = (local_count, group_count, capacity, piece_width)
    route_ids = expert_ids.reshape(-1)
    onehot = (route_ids[:, None] == jnp.arange(expert_total, dtype=jnp.int32)[None, :]).astype(
        jnp.bfloat16
    )
    order = jnp.arange(route_count, dtype=jnp.int32)
    lower = (order[None, :] < order[:, None]).astype(jnp.bfloat16)
    earlier = jnp.dot(lower, onehot, preferred_element_type=jnp.float32)
    slot_rank = jnp.sum(onehot.astype(jnp.float32) * earlier, axis=1).astype(jnp.int32)
    slot_index = (
        route_ids % local_count * rows_all + route_ids // local_count * capacity + slot_rank
    )
    route_hit = slot_index[:, None] == jnp.arange(slot_count, dtype=jnp.int32)[None, :]
    token_hit = jnp.any(route_hit.reshape(tok_count, top_count, slot_count), axis=1).astype(
        jnp.bfloat16
    )
    weight_flat = route_weights.reshape(-1)
    slot_weight = jnp.sum(jnp.where(route_hit, weight_flat[:, None], 0.0), axis=0)
    route_pick = route_hit.astype(jnp.bfloat16)
    outbound = lax.dot_general(
        route_pick,
        jnp.repeat(tokens, top_count, axis=0),
        (((0,), (0,)), ((), ())),
        preferred_element_type=jnp.float32,
    ).astype(jnp.bfloat16)
    grad_outbound = (
        slot_weight[:, None]
        * lax.dot_general(
            route_pick,
            jnp.repeat(out_grad, top_count, axis=0),
            (((0,), (0,)), ((), ())),
            preferred_element_type=jnp.float32,
        )
    ).astype(jnp.bfloat16)
    arrived = lax.all_to_all(
        outbound.reshape(block_shape), "expert", split_axis=1, concat_axis=1, tiled=True
    ).reshape(local_count, rows_all, piece_width)
    preact = lax.psum_scatter(
        jnp.einsum(
            "lrk,lkf->rlf", arrived, gate_up_weight, preferred_element_type=jnp.float32
        ).astype(jnp.bfloat16),
        "dp",
        scatter_dimension=0,
        tiled=True,
    ).astype(jnp.float32)
    grad_arrived = lax.all_to_all(
        grad_outbound.reshape(block_shape), "expert", split_axis=1, concat_axis=1, tiled=True
    ).reshape(local_count, rows_all, piece_width)
    preact, grad_arrived = lax.optimization_barrier((preact, grad_arrived))
    gate_pre = preact[..., :hidden_units]
    up_pre = preact[..., hidden_units:]
    sigmoid_gate = jax.nn.sigmoid(gate_pre)
    activation = gate_pre * sigmoid_gate
    hidden_mine = (activation * up_pre).astype(jnp.bfloat16)
    hidden_mine, grad_arrived = lax.optimization_barrier((hidden_mine, grad_arrived))
    hidden_all = lax.all_gather(hidden_mine, "dp", axis=0, tiled=True)
    hidden_grad_part = jnp.einsum(
        "lrk,lfk->rlf", grad_arrived, down_weight, preferred_element_type=jnp.float32
    ).astype(jnp.bfloat16)
    hidden_grad = lax.psum_scatter(hidden_grad_part, "dp", scatter_dimension=0, tiled=True)
    hidden_all, _ = lax.optimization_barrier((hidden_all, hidden_grad_part))
    out_slice = jnp.einsum(
        "rlf,lfk->lrk", hidden_all, down_weight, preferred_element_type=jnp.float32
    ).astype(jnp.bfloat16)
    hidden_grad = hidden_grad.astype(jnp.float32)
    gate_grad = hidden_grad * up_pre * sigmoid_gate * (1.0 + gate_pre * (1.0 - sigmoid_gate))
    up_grad = hidden_grad * activation
    preact_grad = jnp.concatenate([gate_grad, up_grad], axis=2).astype(jnp.bfloat16)
    preact_grad_all = lax.all_gather(preact_grad, "dp", axis=0, tiled=True)
    grad_routes = jnp.repeat(out_grad, top_count, axis=0).astype(jnp.float32)
    returned = lax.all_to_all(
        out_slice.reshape(block_shape), "expert", split_axis=1, concat_axis=1, tiled=True
    )
    route_pick = route_hit.astype(jnp.bfloat16)
    y_routes = jnp.dot(
        route_pick, returned.reshape(slot_count, piece_width), preferred_element_type=jnp.float32
    )
    layer_out = (
        (weight_flat[:, None] * y_routes)
        .reshape(tok_count, top_count, piece_width)
        .sum(axis=1)
        .astype(jnp.bfloat16)
    )
    partial_dot = jnp.sum(grad_routes * y_routes, axis=1).reshape(tok_count, top_count)
    route_grad = lax.psum(partial_dot, "dp")
    x_grad_slice = jnp.einsum(
        "rlf,lkf->lrk", preact_grad_all, gate_up_weight, preferred_element_type=jnp.float32
    ).astype(jnp.bfloat16)
    gate_up_grad = jnp.einsum(
        "lrk,rlf->lkf", arrived, preact_grad_all, preferred_element_type=jnp.float32
    ).astype(jnp.bfloat16)
    down_grad = jnp.einsum(
        "rlf,lrk->lfk", hidden_all, grad_arrived, preferred_element_type=jnp.float32
    ).astype(jnp.bfloat16)
    grad_back = lax.all_to_all(
        x_grad_slice.reshape(block_shape), "expert", split_axis=1, concat_axis=1, tiled=True
    )
    token_grad = jnp.dot(
        token_hit, grad_back.reshape(slot_count, piece_width), preferred_element_type=jnp.float32
    ).astype(jnp.bfloat16)
    return (layer_out, token_grad, route_grad, gate_up_grad, down_grad)


def solution(mesh):
    placed = (
        P("expert", "dp"),
        P("expert", None),
        P("expert", None),
        P("expert", "dp", None),
        P("expert", None, "dp"),
        P("expert", "dp"),
    )
    return jax.shard_map(
        layer,
        mesh=mesh,
        in_specs=placed,
        out_specs=(
            P("expert", "dp"),
            P("expert", "dp"),
            P("expert", None),
            P("expert", "dp", None),
            P("expert", None, "dp"),
        ),
        check_vma=False,
    )
```
